128 devices in a mesh: ty: 8 (over z, core), tx: 16 (over x, y).
Axes of the slice: x: 4, y: 4, z: 4, core: 2. Of those that a mesh axis runs over, the one named last changes fastest.
Arguments:
- specimen: float32 [2, 8192, 8192], P(None, 'ty', 'tx'), may hold values from -6 to 6
- probe_modes: float32 [2, 3, 512, 512], replicated, may hold values from -6 to 6
- amplitude: float32 [256, 512, 512], P(('ty', 'tx')), may hold values from 0.5 to 3
- offsets: int32 [256, 2], P(('ty', 'tx')), may hold values from 0 to 1023, as said below
- live_slots: int32 [256], P(('ty', 'tx')), may hold values from 0 to 1, as said below
Outputs:
- specimen_grad: float32 [2, 8192, 8192], P(None, 'ty', 'tx')
- probe_grad: float32 [2, 3, 512, 512], replicated
The draws below stay inside these ranges and needn't reach their ends.
Inputs may be any that keep to these rules, and one draw needn't show every extreme that they name: `offsets`: offsets are a row below 1024 and a column below 512 within the tile of the slot's device, chosen so that the 512 x 512 patch lies inside the object. `live_slots`: on each device the live slots come first; the two devices with tx indices 2m and 2m+1 and the same ty index hold exactly 2 live slots together.
All inputs are finite; a program needn't handle non-finite values.
Results may differ from the reference program's by a relative error of at most 0.0038.
The reference program's roundings to bfloat16 on the way count: a program that leaves them out, or rounds other values in their place, can miss the bound.
Values sent between devices are 32-bit elements; how exact they have to be, the bound alone decides.
No kernel may reach another device: no remote copies, remote signals or barrier semaphores. Data moves between devices by JAX's collectives and lax.ppermute only.
A program may use at most 128 MiB of HBM per device.

```python
import math
import jax
import jax.numpy as jnp
from jax import lax

PATCH = 512
MODES = 3
TH = 1024
TW = 512
CAP = 2
OBJ_H = 8192
OBJ_W = 8192
SLOTS = 256
N_TX = 16


def draw_live_slots(key, part):
    devices_all = SLOTS // CAP
    first_count = jax.random.randint(key, (devices_all,), 1, CAP + 1)
    device = jnp.arange(devices_all, dtype=jnp.int32)
    pair_first = device - device % 2
    leader = jnp.where(pair_first == 0, 1, first_count[pair_first])
    leader = jnp.where(pair_first == devices_all - 2, 0, leader)
    holding = jnp.where(device % 2 == 0, leader, CAP - leader)
    slot_index = jnp.arange(SLOTS, dtype=jnp.int32)
    return (slot_index % CAP < holding[slot_index // CAP]).astype(jnp.int32)


def draw_offsets(key, part):
    tile_rows = OBJ_H // TH
    tile_cols = OBJ_W // TW
    slot_index = jnp.arange(SLOTS, dtype=jnp.int32)
    device = slot_index // CAP
    row_limit = jnp.where(device // tile_cols == tile_rows - 1, TH - PATCH + 1, TH)
    col_limit = jnp.where(device % tile_cols == tile_cols - 1, TW - PATCH + 1, TW)
    key_rows = jax.random.fold_in(key, 11)
    key_cols = jax.random.fold_in(key, 23)
    row_at = jax.random.randint(key_rows, (SLOTS,), 0, row_limit)
    col_at = jax.random.randint(key_cols, (SLOTS,), 0, col_limit)
    first_slot = slot_index % CAP == 0
    row_at = jnp.where(first_slot, row_limit - 1, row_at)
    col_at = jnp.where(first_slot, col_limit - 1, col_at)
    return jnp.stack([row_at, col_at], axis=1).astype(jnp.int32)


def shard_levels(rng, shape, pieces, least, top_value):
    factor_of = 1.0
    for axis_at, shards_of in pieces:
        draws = jax.random.uniform(jax.random.fold_in(jax.random.fold_in(rng, 6), axis_at), (shards_of,), jnp.float32, least / len(pieces), top_value / len(pieces))
        factor_of = factor_of * jnp.repeat(jnp.exp(draws), shape[axis_at] // shards_of).reshape((-1,) + (1,) * (len(shape) - 1 - axis_at))
    return factor_of


def normal_values(stream_key, extent, scale, limit, pieces=(), kind=jnp.bfloat16):
    level = shard_levels(stream_key, extent, pieces, -0.22, 0.18) if pieces else 1.0
    result = jax.random.normal(stream_key, extent, jnp.float32) * scale * level
    return jnp.minimum(jnp.maximum(result, -limit), limit).astype(kind)


def setup_inputs(seed: int = 0) -> dict:
    key_list = jax.random.split(jax.random.key(seed), 6)
    return {
        "specimen": normal_values(key_list[0], (2, OBJ_H, OBJ_W), 0.7, 6.0, ((1, 8), (2, 16)), jnp.float32),
        "probe_modes": normal_values(key_list[1], (2, MODES, PATCH, PATCH), 0.6, 6.0, (), jnp.float32),
        "amplitude": jnp.clip(jnp.exp(math.log(3.0) - 1.7917595 * jax.random.uniform(key_list[2], (SLOTS, PATCH, PATCH), jnp.float32) ** shard_levels(key_list[2], (SLOTS, PATCH, PATCH), ((0, 128),), -0.2, 0.2)), 0.5, 3.0),
        "offsets": draw_offsets(jax.random.fold_in(key_list[5], 71), 0),
        "live_slots": draw_live_slots(jax.random.fold_in(key_list[5], 71), 0),
    }


def tables(length):
    index = jnp.arange(length, dtype=jnp.int32)
    phase = index[:, None] * index[None, :] % length
    angle = phase.astype(jnp.float32) * (2.0 * math.pi / length)
    scale = 1.0 / math.sqrt(length)
    return ((jnp.cos(angle) * scale).astype(jnp.bfloat16), (jnp.sin(angle) * scale).astype(jnp.bfloat16))

def left_product(matrix, stacked):
    return jnp.einsum('ij,mjk->mik', matrix.astype(jnp.float32), stacked.astype(jnp.float32))

def right_product(stacked, matrix):
    return jnp.einsum('mij,jk->mik', stacked.astype(jnp.float32), matrix.astype(jnp.float32))

def transform(real_part, imag_part, cos_table, sin_table, orient):
    length = real_part.shape[-1]
    stacked = jnp.concatenate([real_part, imag_part], axis=2)
    cos_part = left_product(cos_table, stacked)
    sin_part = left_product(sin_table, stacked)
    middle_re = (cos_part[:, :, :length] + orient * sin_part[:, :, length:]).astype(jnp.bfloat16)
    middle_im = (cos_part[:, :, length:] - orient * sin_part[:, :, :length]).astype(jnp.bfloat16)
    stacked = jnp.concatenate([middle_re, middle_im], axis=1)
    cos_part = right_product(stacked, cos_table)
    sin_part = right_product(stacked, sin_table)
    result_re = cos_part[:, :length] + orient * sin_part[:, length:]
    result_im = cos_part[:, length:] - orient * sin_part[:, :length]
    return (result_re, result_im)

def slot_terms(window, probe_modes, measured, alive_mask, cos_table, sin_table):
    window_re, window_im = (window[0], window[1])
    probe_re, probe_im = (probe_modes[0], probe_modes[1])
    wave_re = (probe_re * window_re - probe_im * window_im).astype(jnp.bfloat16)
    wave_im = (probe_re * window_im + probe_im * window_re).astype(jnp.bfloat16)
    far_re, far_im = transform(wave_re, wave_im, cos_table, sin_table, 1.0)
    intensity = lax.optimization_barrier(jnp.sum(far_re * far_re + far_im * far_im, axis=0))
    factor = measured * lax.rsqrt(jnp.maximum(intensity, 1.0)) - 1.0
    delta_re = (far_re * factor).astype(jnp.bfloat16)
    delta_im = (far_im * factor).astype(jnp.bfloat16)
    back_re, back_im = transform(delta_re, delta_im, cos_table, sin_table, -1.0)
    back_re = back_re * alive_mask
    back_im = back_im * alive_mask
    grad_re = lax.optimization_barrier(jnp.sum(probe_re * back_re + probe_im * back_im, axis=0))
    grad_im = lax.optimization_barrier(jnp.sum(probe_re * back_im - probe_im * back_re, axis=0))
    mode_re = window_re * back_re + window_im * back_im
    mode_im = window_re * back_im - window_im * back_re
    return (jnp.stack([grad_re, grad_im]), jnp.stack([mode_re, mode_im]))

def reference(specimen, probe_modes, amplitude, offsets, live_slots):
    cos_table, sin_table = tables(PATCH)
    alive_all = live_slots.astype(jnp.float32)
    slot_index = jnp.arange(SLOTS, dtype=jnp.int32)
    device = slot_index // CAP
    row_start = (device // N_TX * TH + offsets[:, 0]).astype(jnp.int32)
    col_start = (device % N_TX * TW + offsets[:, 1]).astype(jnp.int32)
    anchor = jnp.zeros((), jnp.int32)

    def visit(carry, slot_items):
        grad_total, probe_total = carry
        row_at, col_at, measured, alive_mask = slot_items
        window = lax.dynamic_slice(specimen, (anchor, row_at, col_at), (2, PATCH, PATCH))
        grad_term, probe_term = slot_terms(window, probe_modes, measured, alive_mask, cos_table, sin_table)
        current = lax.dynamic_slice(grad_total, (anchor, row_at, col_at), (2, PATCH, PATCH))
        grad_total = lax.dynamic_update_slice(grad_total, current + grad_term, (anchor, row_at, col_at))
        return ((grad_total, probe_total + probe_term), None)
    start = (jnp.zeros(specimen.shape, jnp.float32), jnp.zeros(probe_modes.shape, jnp.float32))
    (grad_total, probe_total), _ = lax.scan(visit, start, (row_start, col_start, amplitude, alive_all))
    return (grad_total, probe_total * (1.0 / math.sqrt(SLOTS)))
```

```python
import math

import jax
import jax.numpy as jnp
from jax import lax
from jax.sharding import Mesh
from jax.sharding import PartitionSpec as P

TY = ("ty_0", "ty_1")
TX = ("tx_0", "tx_1")
TY_TX = ("ty_0", "ty_1", "tx_0", "tx_1")


def passed_along(value, axis, steps):
    count = lax.axis_size(axis)
    initial, last = (max(0, -steps), min(count, count - steps))
    return lax.ppermute(value, axis, [(source, source + steps) for source in range(initial, last)])


def partner(value, axis, apart):
    mask = 2**apart
    pairs = [(source, source ^ mask) for source in range(lax.axis_size(axis))]
    return lax.ppermute(value, axis, pairs)


def filled_up(lines, devices):
    spare = -len(lines) % devices
    return jnp.pad(lines, [(0, spare)] + [(0, 0)] * (lines.ndim - 1))


def sum_in_order(parts, axes, sequence):
    dims = [lax.axis_size(a) for a in axes]
    parts = parts.reshape(*dims, *parts.shape[1:])
    parts = parts.transpose(*sequence, *range(len(axes), parts.ndim))
    parts = parts.reshape(-1, *parts.shape[len(axes) :])
    for k in sequence:
        parts = lax.psum_scatter(parts, axes[k], scatter_dimension=0, tiled=True)
    return parts[0]


def gather_in_order(shard, axes, sequence):
    parts = shard
    for k in sequence:
        parts = lax.all_gather(parts, axes[k])
    done = sequence[::-1]
    back = [done.index(k) for k in range(len(axes))]
    parts = parts.transpose(*back, *range(len(axes), parts.ndim))
    return parts.reshape(-1, *shard.shape)


def sum_in_two_steps(shard, axes, sequence):
    devices, lines = (lax.axis_size(axes), shard.reshape(-1, *shard.shape[1:][-1:]))
    parts = filled_up(lines, devices).reshape(devices, -1, *lines.shape[1:])
    own = sum_in_order(parts, axes, sequence)
    whole = gather_in_order(own, axes, sequence[::-1]).reshape(-1, *lines.shape[1:])
    return whole[: len(lines)].reshape(shard.shape)


def scatter_axis(lines, axis):
    count = lax.axis_size(axis)
    me = lax.axis_index(axis)
    chunks = lines.reshape(count, -1, lines.shape[-1])
    total = lax.dynamic_index_in_dim(chunks, me, keepdims=False)
    for step in range(1, count):
        sent = lax.dynamic_index_in_dim(chunks, (me + step) % count, keepdims=False)
        pairs = [(source, (source + step) % count) for source in range(count)]
        total = total + lax.ppermute(sent, axis, pairs)
    return total


def gather_axis(piece, axis):
    count = lax.axis_size(axis)
    me = lax.axis_index(axis)
    whole = jnp.zeros((count,) + piece.shape, piece.dtype)
    whole = lax.dynamic_update_index_in_dim(whole, piece, me, 0)
    for step in range(1, count):
        pairs = [(source, (source + step) % count) for source in range(count)]
        got = lax.ppermute(piece, axis, pairs)
        whole = lax.dynamic_update_index_in_dim(whole, got, (me - step) % count, 0)
    return whole.reshape(-1, piece.shape[-1])


def all_sum(value, axes, scale):
    lines = value.reshape(-1, value.shape[-1])
    for axis in axes:
        lines = scatter_axis(lines, axis)
    lines = lines * scale
    for axis in axes[::-1]:
        lines = gather_axis(lines, axis)
    return lines.reshape(value.shape)


def tables(length):
    index = jnp.arange(length, dtype=jnp.int32)
    phase = index[:, None] * index[None, :] % length
    angle = phase.astype(jnp.float32) * (2.0 * math.pi / length)
    scale = 1.0 / math.sqrt(length)
    return (
        (jnp.cos(angle) * scale).astype(jnp.bfloat16),
        (jnp.sin(angle) * scale).astype(jnp.bfloat16),
    )


def transform(real_part, imag_part, cos_table, sin_table, orient):
    length = real_part.shape[-1]
    stacked = jnp.concatenate([real_part, imag_part], axis=2)
    cos_part = jnp.einsum("ij,mjk->mik", cos_table, stacked, preferred_element_type=jnp.float32)
    sin_part = jnp.einsum("ij,mjk->mik", sin_table, stacked, preferred_element_type=jnp.float32)
    middle_re = (cos_part[:, :, :length] + orient * sin_part[:, :, length:]).astype(jnp.bfloat16)
    middle_im = (cos_part[:, :, length:] - orient * sin_part[:, :, :length]).astype(jnp.bfloat16)
    stacked = jnp.concatenate([middle_re, middle_im], axis=1)
    cos_part = jnp.einsum("mij,jk->mik", stacked, cos_table, preferred_element_type=jnp.float32)
    sin_part = jnp.einsum("mij,jk->mik", stacked, sin_table, preferred_element_type=jnp.float32)
    result_re = cos_part[:, :length] + orient * sin_part[:, length:]
    result_im = cos_part[:, length:] - orient * sin_part[:, :length]
    return (result_re, result_im)


def slot_terms(window, probe_modes, measured, alive_mask, cos_table, sin_table):
    window_re, window_im = (window[0], window[1])
    probe_re, probe_im = (probe_modes[0], probe_modes[1])
    wave_re = (probe_re * window_re - probe_im * window_im).astype(jnp.bfloat16)
    wave_im = (probe_re * window_im + probe_im * window_re).astype(jnp.bfloat16)
    far_re, far_im = transform(wave_re, wave_im, cos_table, sin_table, 1.0)
    intensity = jnp.sum(far_re * far_re + far_im * far_im, axis=0)
    factor = measured * lax.rsqrt(jnp.maximum(intensity, 1.0)) - 1.0
    delta_re = (far_re * factor).astype(jnp.bfloat16)
    delta_im = (far_im * factor).astype(jnp.bfloat16)
    back_re, back_im = transform(delta_re, delta_im, cos_table, sin_table, -1.0)
    back_re = back_re * alive_mask
    back_im = back_im * alive_mask
    grad_re = jnp.sum(probe_re * back_re + probe_im * back_im, axis=0)
    grad_im = jnp.sum(probe_re * back_im - probe_im * back_re, axis=0)
    mode_re = window_re * back_re + window_im * back_im
    mode_im = window_re * back_im - window_im * back_re
    return (jnp.stack([grad_re, grad_im]), jnp.stack([mode_re, mode_im]))


def local(specimen, probe_modes, amplitude, offsets, live_slots):
    tile_h = specimen.shape[1]
    tile_w = specimen.shape[2]
    width = probe_modes.shape[2]
    slots = live_slots.shape[0]
    devices_all = lax.axis_size(TY) * lax.axis_size(TX)
    anchor = jnp.zeros((), jnp.int32)
    right_top = passed_along(specimen[:, :width, :], TX, -1)
    later_rows, right_top = lax.optimization_barrier((specimen[:, width:, :], right_top))
    right_bottom = passed_along(later_rows, TX, -1)
    below_own = passed_along(specimen[:, :width, :], TY, -1)
    below_right = passed_along(right_top, TY, -1)
    upper_rows = jnp.concatenate(
        [specimen, jnp.concatenate([right_top, right_bottom], axis=1)], axis=2
    )
    lower_rows = jnp.concatenate([below_own, below_right], axis=2)
    extended = jnp.concatenate([upper_rows, lower_rows], axis=1)
    cos_table, sin_table = tables(width)

    def crop(row_at, col_at):
        return lax.dynamic_slice(extended, (anchor, row_at, col_at), (2, width, width))

    windows = jnp.stack([crop(offsets[k, 0], offsets[k, 1]) for k in range(slots)])
    alive_own = live_slots.astype(jnp.float32)

    def process(slot_items):
        window, measured, alive_mask = slot_items
        return slot_terms(window, probe_modes, measured, alive_mask, cos_table, sin_table)

    half_slots = slots // 2
    live_count = jnp.sum(alive_own)
    got_windows, got_measured, got_count = partner(
        (windows[half_slots:], amplitude[half_slots:], live_count), TX, 0
    )
    position = jnp.arange(half_slots, dtype=jnp.int32)
    taken = jnp.minimum(live_count, float(half_slots)).astype(jnp.int32)
    got_alive = ((position + half_slots).astype(jnp.float32) < got_count).astype(jnp.float32)
    pool_windows = jnp.concatenate([windows[:half_slots], got_windows], axis=0)
    pool_measured = jnp.concatenate([amplitude[:half_slots], got_measured], axis=0)
    pool_alive = jnp.concatenate([alive_own[:half_slots], got_alive], axis=0)
    order_index = jnp.where(position < taken, position, half_slots + position - taken)
    work_windows = jnp.take(pool_windows, order_index, axis=0)
    work_measured = jnp.take(pool_measured, order_index, axis=0)
    work_alive = jnp.take(pool_alive, order_index, axis=0)
    grad_terms, probe_terms = lax.map(process, (work_windows, work_measured, work_alive))
    padded_terms = jnp.concatenate([grad_terms, jnp.zeros_like(grad_terms)], axis=0)
    returned = jnp.take(padded_terms, taken + position, axis=0)
    got_back = partner(returned, TX, 0)
    kept = jnp.where((position < taken)[:, None, None, None], grad_terms, 0.0)
    own_terms = jnp.concatenate([kept, got_back], axis=0)
    probe_grad = all_sum(
        jnp.sum(probe_terms, axis=0), ("ty_1", "ty_0", "tx_0", "tx_1"), 1.0 / math.sqrt(slots * devices_all)
    )

    def place(slot_index, grad_ext):
        row_at = offsets[slot_index, 0]
        col_at = offsets[slot_index, 1]
        current = lax.dynamic_slice(grad_ext, (anchor, row_at, col_at), (2, width, width))
        return lax.dynamic_update_slice(
            grad_ext, current + own_terms[slot_index], (anchor, row_at, col_at)
        )

    grad_ext = jnp.zeros(extended.shape, jnp.float32)
    for k in range(slots):
        grad_ext = place(k, grad_ext)
    corner_above = passed_along(grad_ext[:, tile_h:, tile_w:], TY, 1)
    below_part, corner_above = lax.optimization_barrier((grad_ext[:, tile_h:, :tile_w], corner_above))
    below_above = passed_along(below_part, TY, 1)
    left_bottom = passed_along(grad_ext[:, width:tile_h, tile_w:], TX, 1)
    left_top = passed_along(grad_ext[:, :width, tile_w:] + corner_above, TX, 1)
    top = (grad_ext[:, :width, :tile_w] + below_above).at[:, :, :width].add(left_top)
    bottom = grad_ext[:, width:tile_h, :tile_w].at[:, :, :width].add(left_bottom)
    core_grad = jnp.concatenate([top, bottom], axis=1)
    return (core_grad, probe_grad)


def solution(mesh):
    finer = Mesh(mesh.devices.reshape(4, 2, 4, 4), ("ty_0", "ty_1", "tx_0", "tx_1"))
    placed = (P(None, TY, TX), P(), P(TY_TX, None, None), P(TY_TX, None), P(TY_TX))
    return jax.shard_map(
        local, mesh=finer, in_specs=placed, out_specs=(P(None, TY, TX), P()), check_vma=False
    )
```

```python
import math

import jax
import jax.numpy as jnp
from jax import lax
from jax.sharding import Mesh
from jax.sharding import PartitionSpec as P

TY = ("ty_0", "ty_1")
TX = ("tx_0", "tx_1")
TY_TX = ("ty_0", "ty_1", "tx_0", "tx_1")


def passed_along(value, axis, steps):
    count = lax.axis_size(axis)
    initial, last = (max(0, -steps), min(count, count - steps))
    return lax.ppermute(value, axis, [(source, source + steps) for source in range(initial, last)])


def partner(value, axis, apart):
    mask = 2**apart
    pairs = [(source, source ^ mask) for source in range(lax.axis_size(axis))]
    return lax.ppermute(value, axis, pairs)


def filled_up(lines, devices):
    spare = -len(lines) % devices
    return jnp.pad(lines, [(0, spare)] + [(0, 0)] * (lines.ndim - 1))


def sum_in_order(parts, axes, sequence):
    dims = [lax.axis_size(a) for a in axes]
    parts = parts.reshape(*dims, *parts.shape[1:])
    parts = parts.transpose(*sequence, *range(len(axes), parts.ndim))
    parts = parts.reshape(-1, *parts.shape[len(axes) :])
    for k in sequence:
        parts = lax.psum_scatter(parts, axes[k], scatter_dimension=0, tiled=True)
    return parts[0]


def gather_in_order(shard, axes, sequence):
    parts = shard
    for k in sequence:
        parts = lax.all_gather(parts, axes[k])
    done = sequence[::-1]
    back = [done.index(k) for k in range(len(axes))]
    parts = parts.transpose(*back, *range(len(axes), parts.ndim))
    return parts.reshape(-1, *shard.shape)


def sum_in_two_steps(shard, axes, sequence):
    devices, lines = (lax.axis_size(axes), shard.reshape(-1, *shard.shape[1:][-1:]))
    parts = filled_up(lines, devices).reshape(devices, -1, *lines.shape[1:])
    own = sum_in_order(parts, axes, sequence)
    whole = gather_in_order(own, axes, sequence[::-1]).reshape(-1, *lines.shape[1:])
    return whole[: len(lines)].reshape(shard.shape)


def scatter_axis(lines, axis):
    count = lax.axis_size(axis)
    me = lax.axis_index(axis)
    chunks = lines.reshape(count, -1, lines.shape[-1])
    total = lax.dynamic_index_in_dim(chunks, me, keepdims=False)
    for step in range(1, count):
        sent = lax.dynamic_index_in_dim(chunks, (me + step) % count, keepdims=False)
        pairs = [(source, (source + step) % count) for source in range(count)]
        total = total + lax.ppermute(sent, axis, pairs)
    return total


def gather_axis(piece, axis):
    count = lax.axis_size(axis)
    me = lax.axis_index(axis)
    whole = jnp.zeros((count,) + piece.shape, piece.dtype)
    whole = lax.dynamic_update_index_in_dim(whole, piece, me, 0)
    for step in range(1, count):
        pairs = [(source, (source + step) % count) for source in range(count)]
        got = lax.ppermute(piece, axis, pairs)
        whole = lax.dynamic_update_index_in_dim(whole, got, (me - step) % count, 0)
    return whole.reshape(-1, piece.shape[-1])


def all_sum(value, axes, scale):
    lines = value.reshape(-1, value.shape[-1])
    for axis in axes:
        lines = scatter_axis(lines, axis)
    lines = lines * scale
    for axis in axes[::-1]:
        lines = gather_axis(lines, axis)
    return lines.reshape(value.shape)


def tables(length):
    index = jnp.arange(length, dtype=jnp.int32)
    phase = index[:, None] * index[None, :] % length
    angle = phase.astype(jnp.float32) * (2.0 * math.pi / length)
    scale = 1.0 / math.sqrt(length)
    return (
        (jnp.cos(angle) * scale).astype(jnp.bfloat16),
        (jnp.sin(angle) * scale).astype(jnp.bfloat16),
    )


def transform(real_part, imag_part, cos_table, sin_table, orient):
    length = real_part.shape[-1]
    stacked = jnp.concatenate([real_part, imag_part], axis=2)
    cos_part = jnp.einsum("ij,mjk->mik", cos_table, stacked, preferred_element_type=jnp.float32)
    sin_part = jnp.einsum("ij,mjk->mik", sin_table, stacked, preferred_element_type=jnp.float32)
    middle_re = (cos_part[:, :, :length] + orient * sin_part[:, :, length:]).astype(jnp.bfloat16)
    middle_im = (cos_part[:, :, length:] - orient * sin_part[:, :, :length]).astype(jnp.bfloat16)
    stacked = jnp.concatenate([middle_re, middle_im], axis=1)
    cos_part = jnp.einsum("mij,jk->mik", stacked, cos_table, preferred_element_type=jnp.float32)
    sin_part = jnp.einsum("mij,jk->mik", stacked, sin_table, preferred_element_type=jnp.float32)
    result_re = cos_part[:, :length] + orient * sin_part[:, length:]
    result_im = cos_part[:, length:] - orient * sin_part[:, :length]
    return (result_re, result_im)


def slot_terms(window, probe_modes, measured, alive_mask, cos_table, sin_table):
    window_re, window_im = (window[0], window[1])
    probe_re, probe_im = (probe_modes[0], probe_modes[1])
    wave_re = (probe_re * window_re - probe_im * window_im).astype(jnp.bfloat16)
    wave_im = (probe_re * window_im + probe_im * window_re).astype(jnp.bfloat16)
    far_re, far_im = transform(wave_re, wave_im, cos_table, sin_table, 1.0)
    intensity = jnp.sum(far_re * far_re + far_im * far_im, axis=0)
    factor = measured * lax.rsqrt(jnp.maximum(intensity, 1.0)) - 1.0
    delta_re = (far_re * factor).astype(jnp.bfloat16)
    delta_im = (far_im * factor).astype(jnp.bfloat16)
    back_re, back_im = transform(delta_re, delta_im, cos_table, sin_table, -1.0)
    back_re = back_re * alive_mask
    back_im = back_im * alive_mask
    grad_re = jnp.sum(probe_re * back_re + probe_im * back_im, axis=0)
    grad_im = jnp.sum(probe_re * back_im - probe_im * back_re, axis=0)
    mode_re = window_re * back_re + window_im * back_im
    mode_im = window_re * back_im - window_im * back_re
    return (jnp.stack([grad_re, grad_im]), jnp.stack([mode_re, mode_im]))


def shifted(value, axis, pairs):
    return lax.ppermute(value, axis, [(a, b) for a, b in pairs if 0 <= b < lax.axis_size(axis)])


def local(specimen, probe_modes, amplitude, offsets, live_slots):
    tile_h = specimen.shape[1]
    width = probe_modes.shape[2]
    slots = live_slots.shape[0]
    devices_all = lax.axis_size(TY) * lax.axis_size(TX)
    count = lax.axis_size(TX)
    evens = range(0, count, 2)
    odds = range(1, count, 2)
    anchor = jnp.zeros((), jnp.int32)
    cos_table, sin_table = tables(width)

    alive_own = live_slots.astype(jnp.float32)
    live_count = jnp.sum(alive_own)
    got_measured, got_count, got_offset = partner((amplitude[1:], live_count, offsets[1]), TX, 0)
    use_own = live_count >= 1.0
    is_odd = lax.axis_index(TX) % 2 == 1
    shift = jnp.where(use_own, 0, jnp.where(is_odd, -1, 1))
    row_at = jnp.where(use_own, offsets[0, 0], got_offset[0])
    col_at = jnp.where(use_own, offsets[0, 1], got_offset[1])
    measured = jnp.where(use_own, amplitude[0], got_measured[0])
    alive = jnp.where(use_own, alive_own[0], (1.0 < got_count).astype(jnp.float32))

    row_left = shifted(row_at, TX, [(s, s + 1) for s in range(count)])
    row_right = shifted(row_at, TX, [(s, s - 1) for s in range(count)])
    row_left2 = shifted(row_at, TX, [(s, s + 2) for s in evens])

    below = passed_along(specimen[:, :width, :], TY, -1)
    column = jnp.concatenate([specimen, below], axis=1)

    def strip(source, at):
        return lax.dynamic_slice(source, (anchor, at, anchor), (2, width, width))

    own_strip = strip(column, row_at)
    from_right = shifted(strip(column, row_left), TX, [(s, s - 1) for s in range(count)])
    from_left = shifted(strip(column, row_right), TX, [(s, s + 1) for s in evens])
    from_right2 = shifted(strip(column, row_left2), TX, [(s, s - 2) for s in evens])
    left_strip = jnp.where(shift == 0, own_strip, jnp.where(shift < 0, from_left, from_right))
    right_strip = jnp.where(shift == 0, from_right, jnp.where(shift < 0, own_strip, from_right2))
    pair_strip = jnp.concatenate([left_strip, right_strip], axis=2)
    window = lax.dynamic_slice(pair_strip, (anchor, anchor, col_at), (2, width, width))

    grad_term, probe_term = slot_terms(window, probe_modes, measured, alive, cos_table, sin_table)

    probe_grad = all_sum(probe_term, ("ty_1", "ty_0", "tx_0", "tx_1"), 1.0 / math.sqrt(slots * devices_all))

    placed = lax.dynamic_update_slice(
        jnp.zeros((2, width, 2 * width), jnp.float32), grad_term, (anchor, anchor, col_at)
    )
    grad_left = placed[:, :, :width]
    grad_right = placed[:, :, width:]
    zeros = jnp.zeros_like(grad_left)
    send_right = jnp.where(shift == 0, grad_right, jnp.where(shift > 0, grad_left, zeros))
    send_right2 = jnp.where(shift > 0, grad_right, zeros)
    send_left = jnp.where(shift < 0, grad_left, zeros)
    keep = jnp.where(shift == 0, grad_left, jnp.where(shift < 0, grad_right, zeros))
    got_left = shifted(send_right, TX, [(s, s + 1) for s in range(count)])
    got_left2 = shifted(send_right2, TX, [(s, s + 2) for s in evens])
    got_right = shifted(send_left, TX, [(s, s - 1) for s in odds])

    def add_strip(total, piece, at):
        current = lax.dynamic_slice(total, (anchor, at, anchor), (2, width, width))
        return lax.dynamic_update_slice(total, current + piece, (anchor, at, anchor))

    grad_column = jnp.zeros(column.shape, jnp.float32)
    grad_column = add_strip(grad_column, keep, row_at)
    grad_column = add_strip(grad_column, got_left, row_left)
    grad_column = add_strip(grad_column, got_left2, row_left2)
    grad_column = add_strip(grad_column, got_right, row_right)
    from_above = passed_along(grad_column[:, tile_h:, :], TY, 1)
    core_grad = grad_column[:, :tile_h, :].at[:, :width, :].add(from_above)
    return (core_grad, probe_grad)


def solution(mesh):
    finer = Mesh(mesh.devices.reshape(4, 2, 4, 4), ("ty_0", "ty_1", "tx_0", "tx_1"))
    placed = (P(None, TY, TX), P(), P(TY_TX, None, None), P(TY_TX, None), P(TY_TX))
    return jax.shard_map(
        local, mesh=finer, in_specs=placed, out_specs=(P(None, TY, TX), P()), check_vma=False
    )
```

```python
import math

import jax
import jax.numpy as jnp
from jax import lax
from jax.sharding import Mesh
from jax.sharding import PartitionSpec as P

TY = ("ty_0", "ty_1")
TX = ("tx_0", "tx_1")
TY_TX = ("ty_0", "ty_1", "tx_0", "tx_1")


def passed_along(value, axis, steps):
    count = lax.axis_size(axis)
    initial, last = (max(0, -steps), min(count, count - steps))
    return lax.ppermute(value, axis, [(source, source + steps) for source in range(initial, last)])


def partner(value, axis, apart):
    mask = 2**apart
    pairs = [(source, source ^ mask) for source in range(lax.axis_size(axis))]
    return lax.ppermute(value, axis, pairs)


def filled_up(lines, devices):
    spare = -len(lines) % devices
    return jnp.pad(lines, [(0, spare)] + [(0, 0)] * (lines.ndim - 1))


def sum_in_order(parts, axes, sequence):
    dims = [lax.axis_size(a) for a in axes]
    parts = parts.reshape(*dims, *parts.shape[1:])
    parts = parts.transpose(*sequence, *range(len(axes), parts.ndim))
    parts = parts.reshape(-1, *parts.shape[len(axes) :])
    for k in sequence:
        parts = lax.psum_scatter(parts, axes[k], scatter_dimension=0, tiled=True)
    return parts[0]


def gather_in_order(shard, axes, sequence):
    parts = shard
    for k in sequence:
        parts = lax.all_gather(parts, axes[k])
    done = sequence[::-1]
    back = [done.index(k) for k in range(len(axes))]
    parts = parts.transpose(*back, *range(len(axes), parts.ndim))
    return parts.reshape(-1, *shard.shape)


def sum_in_two_steps(shard, axes, sequence):
    devices, lines = (lax.axis_size(axes), shard.reshape(-1, *shard.shape[1:][-1:]))
    parts = filled_up(lines, devices).reshape(devices, -1, *lines.shape[1:])
    own = sum_in_order(parts, axes, sequence)
    whole = gather_in_order(own, axes, sequence[::-1]).reshape(-1, *lines.shape[1:])
    return whole[: len(lines)].reshape(shard.shape)


def scatter_axis(lines, axis):
    count = lax.axis_size(axis)
    me = lax.axis_index(axis)
    chunks = lines.reshape(count, -1, lines.shape[-1])
    total = lax.dynamic_index_in_dim(chunks, me, keepdims=False)
    for step in range(1, count):
        sent = lax.dynamic_index_in_dim(chunks, (me + step) % count, keepdims=False)
        pairs = [(source, (source + step) % count) for source in range(count)]
        total = total + lax.ppermute(sent, axis, pairs)
    return total


def gather_axis(piece, axis):
    count = lax.axis_size(axis)
    me = lax.axis_index(axis)
    whole = jnp.zeros((count,) + piece.shape, piece.dtype)
    whole = lax.dynamic_update_index_in_dim(whole, piece, me, 0)
    for step in range(1, count):
        pairs = [(source, (source + step) % count) for source in range(count)]
        got = lax.ppermute(piece, axis, pairs)
        whole = lax.dynamic_update_index_in_dim(whole, got, (me - step) % count, 0)
    return whole.reshape(-1, piece.shape[-1])


def all_sum(value, axes, scale):
    lines = value.reshape(-1, value.shape[-1])
    for axis in axes:
        lines = scatter_axis(lines, axis)
    lines = lines * scale
    for axis in axes[::-1]:
        lines = gather_axis(lines, axis)
    return lines.reshape(value.shape)


def tables(length):
    index = jnp.arange(length, dtype=jnp.int32)
    phase = index[:, None] * index[None, :] % length
    angle = phase.astype(jnp.float32) * (2.0 * math.pi / length)
    scale = 1.0 / math.sqrt(length)
    return (
        (jnp.cos(angle) * scale).astype(jnp.bfloat16),
        (jnp.sin(angle) * scale).astype(jnp.bfloat16),
    )


def transform(real_part, imag_part, cos_table, sin_table, orient):
    length = real_part.shape[-1]
    stacked = jnp.concatenate([real_part, imag_part], axis=2)
    cos_part = jnp.einsum("ij,mjk->mik", cos_table, stacked, preferred_element_type=jnp.float32)
    sin_part = jnp.einsum("ij,mjk->mik", sin_table, stacked, preferred_element_type=jnp.float32)
    middle_re = (cos_part[:, :, :length] + orient * sin_part[:, :, length:]).astype(jnp.bfloat16)
    middle_im = (cos_part[:, :, length:] - orient * sin_part[:, :, :length]).astype(jnp.bfloat16)
    stacked = jnp.concatenate([middle_re, middle_im], axis=1)
    cos_part = jnp.einsum("mij,jk->mik", stacked, cos_table, preferred_element_type=jnp.float32)
    sin_part = jnp.einsum("mij,jk->mik", stacked, sin_table, preferred_element_type=jnp.float32)
    result_re = cos_part[:, :length] + orient * sin_part[:, length:]
    result_im = cos_part[:, length:] - orient * sin_part[:, :length]
    return (result_re, result_im)


def slot_terms(window, probe_modes, measured, alive_mask, cos_table, sin_table):
    window_re, window_im = (window[0], window[1])
    probe_re, probe_im = (probe_modes[0], probe_modes[1])
    wave_re = (probe_re * window_re - probe_im * window_im).astype(jnp.bfloat16)
    wave_im = (probe_re * window_im + probe_im * window_re).astype(jnp.bfloat16)
    far_re, far_im = transform(wave_re, wave_im, cos_table, sin_table, 1.0)
    intensity = jnp.sum(far_re * far_re + far_im * far_im, axis=0)
    factor = measured * lax.rsqrt(jnp.maximum(intensity, 1.0)) - 1.0
    delta_re = (far_re * factor).astype(jnp.bfloat16)
    delta_im = (far_im * factor).astype(jnp.bfloat16)
    back_re, back_im = transform(delta_re, delta_im, cos_table, sin_table, -1.0)
    back_re = back_re * alive_mask
    back_im = back_im * alive_mask
    grad_re = jnp.sum(probe_re * back_re + probe_im * back_im, axis=0)
    grad_im = jnp.sum(probe_re * back_im - probe_im * back_re, axis=0)
    mode_re = window_re * back_re + window_im * back_im
    mode_im = window_re * back_im - window_im * back_re
    return (jnp.stack([grad_re, grad_im]), jnp.stack([mode_re, mode_im]))


def shifted(value, axis, pairs):
    return lax.ppermute(value, axis, [(a, b) for a, b in pairs if 0 <= b < lax.axis_size(axis)])


def local(specimen, probe_modes, amplitude, offsets, live_slots):
    tile_h = specimen.shape[1]
    width = probe_modes.shape[2]
    slots = live_slots.shape[0]
    devices_all = lax.axis_size(TY) * lax.axis_size(TX)
    count = lax.axis_size(TX)
    evens = range(0, count, 2)
    odds = range(1, count, 2)
    anchor = jnp.zeros((), jnp.int32)
    cos_table, sin_table = tables(width)

    alive_own = live_slots.astype(jnp.float32)
    live_count = jnp.sum(alive_own)
    got_measured, got_count, got_offset = partner((amplitude[1:], live_count, offsets[1]), TX, 0)
    use_own = live_count >= 1.0
    is_odd = lax.axis_index(TX) % 2 == 1
    shift = jnp.where(use_own, 0, jnp.where(is_odd, -1, 1))
    row_at = jnp.where(use_own, offsets[0, 0], got_offset[0])
    col_at = jnp.where(use_own, offsets[0, 1], got_offset[1])
    measured = jnp.where(use_own, amplitude[0], got_measured[0])
    alive = jnp.where(use_own, alive_own[0], (1.0 < got_count).astype(jnp.float32))

    row_left = shifted(row_at, TX, [(s, s + 1) for s in range(count)])
    row_right = shifted(row_at, TX, [(s, s - 1) for s in range(count)])
    row_left2 = shifted(row_at, TX, [(s, s + 2) for s in evens])

    below = passed_along(specimen[:, :width, :], TY, -1)
    column = jnp.concatenate([specimen, below], axis=1)

    def strip(source, at):
        return lax.dynamic_slice(source, (anchor, at, anchor), (2, width, width))

    own_strip = strip(column, row_at)
    from_right = shifted(strip(column, row_left), TX, [(s, s - 1) for s in range(count)])
    from_left = shifted(strip(column, row_right), TX, [(s, s + 1) for s in evens])
    from_right2 = shifted(strip(column, row_left2), TX, [(s, s - 2) for s in evens])
    left_strip = jnp.where(shift == 0, own_strip, jnp.where(shift < 0, from_left, from_right))
    right_strip = jnp.where(shift == 0, from_right, jnp.where(shift < 0, own_strip, from_right2))
    pair_strip = jnp.concatenate([left_strip, right_strip], axis=2)
    window = lax.dynamic_slice(pair_strip, (anchor, anchor, col_at), (2, width, width))

    grad_term, probe_term = slot_terms(window, probe_modes, measured, alive, cos_table, sin_table)

    probe_grad = all_sum(probe_term, ("ty_1", "ty_0", "tx_0", "tx_1"), 1.0 / math.sqrt(slots * devices_all))

    placed = lax.dynamic_slice(
        jnp.pad(grad_term, ((0, 0), (0, 0), (width, width))), (anchor, anchor, width - col_at), (2, width, 2 * width)
    )
    grad_left = placed[:, :, :width]
    grad_right = placed[:, :, width:]
    zeros = jnp.zeros_like(grad_left)
    send_right = jnp.where(shift == 0, grad_right, jnp.where(shift > 0, grad_left, zeros))
    send_right2 = jnp.where(shift > 0, grad_right, zeros)
    send_left = jnp.where(shift < 0, grad_left, zeros)
    keep = jnp.where(shift == 0, grad_left, jnp.where(shift < 0, grad_right, zeros))
    got_left = shifted(send_right, TX, [(s, s + 1) for s in range(count)])
    got_left2 = shifted(send_right2, TX, [(s, s + 2) for s in evens])
    got_right = shifted(send_left, TX, [(s, s - 1) for s in odds])

    rows_all = column.shape[1]

    def spread(piece, at):
        padded = jnp.pad(piece, ((0, 0), (rows_all, rows_all), (0, 0)))
        return lax.dynamic_slice(padded, (anchor, rows_all - at, anchor), (2, rows_all, width))

    grad_column = (
        (spread(keep, row_at) + spread(got_left, row_left)) + spread(got_left2, row_left2)
    ) + spread(got_right, row_right)
    from_above = passed_along(grad_column[:, tile_h:, :], TY, 1)
    core_grad = grad_column[:, :tile_h, :].at[:, :width, :].add(from_above)
    return (core_grad, probe_grad)


def solution(mesh):
    finer = Mesh(mesh.devices.reshape(4, 2, 4, 4), ("ty_0", "ty_1", "tx_0", "tx_1"))
    placed = (P(None, TY, TX), P(), P(TY_TX, None, None), P(TY_TX, None), P(TY_TX))
    return jax.shard_map(
        local, mesh=finer, in_specs=placed, out_specs=(P(None, TY, TX), P()), check_vma=False
    )
```

```python
import math

import jax
import jax.numpy as jnp
from jax import lax
from jax.sharding import Mesh
from jax.sharding import PartitionSpec as P


TY = ("ty_0", "ty_1")
TX = ("tx_0", "tx_1")
TY_TX = ("ty_0", "ty_1", "tx_0", "tx_1")


def passed_along(value, axis, steps):
    count = lax.axis_size(axis)
    initial, last = (max(0, -steps), min(count, count - steps))
    return lax.ppermute(value, axis, [(source, source + steps) for source in range(initial, last)])


def partner(value, axis, apart):
    mask = 2**apart
    pairs = [(source, source ^ mask) for source in range(lax.axis_size(axis))]
    return lax.ppermute(value, axis, pairs)


def scatter_axis(lines, axis):
    count = lax.axis_size(axis)
    me = lax.axis_index(axis)
    chunks = lines.reshape(count, -1, lines.shape[-1])
    total = lax.dynamic_index_in_dim(chunks, me, keepdims=False)
    for step in range(1, count):
        sent = lax.dynamic_index_in_dim(chunks, (me + step) % count, keepdims=False)
        pairs = [(source, (source + step) % count) for source in range(count)]
        total = total + lax.ppermute(sent, axis, pairs)
    return total


def gather_axis(piece, axis):
    count = lax.axis_size(axis)
    me = lax.axis_index(axis)
    whole = jnp.zeros((count,) + piece.shape, piece.dtype)
    whole = lax.dynamic_update_index_in_dim(whole, piece, me, 0)
    for step in range(1, count):
        pairs = [(source, (source + step) % count) for source in range(count)]
        got = lax.ppermute(piece, axis, pairs)
        whole = lax.dynamic_update_index_in_dim(whole, got, (me - step) % count, 0)
    return whole.reshape(-1, piece.shape[-1])


def all_sum(value, axes, scale):
    lines = value.reshape(-1, value.shape[-1])
    for axis in axes:
        lines = scatter_axis(lines, axis)
    lines = lines * scale
    for axis in axes[::-1]:
        lines = gather_axis(lines, axis)
    return lines.reshape(value.shape)


def tables(length):
    index = jnp.arange(length, dtype=jnp.int32)
    phase = index[:, None] * index[None, :] % length
    angle = phase.astype(jnp.float32) * (2.0 * math.pi / length)
    scale = 1.0 / math.sqrt(length)
    return (
        (jnp.cos(angle) * scale).astype(jnp.bfloat16),
        (jnp.sin(angle) * scale).astype(jnp.bfloat16),
    )


def transform(real_part, imag_part, cos_table, sin_table, orient):
    length = real_part.shape[-1]
    stacked = jnp.concatenate([real_part, imag_part], axis=2)
    cos_part = jnp.einsum("ij,mjk->mik", cos_table, stacked, preferred_element_type=jnp.float32)
    sin_part = jnp.einsum("ij,mjk->mik", sin_table, stacked, preferred_element_type=jnp.float32)
    middle_re = (cos_part[:, :, :length] + orient * sin_part[:, :, length:]).astype(jnp.bfloat16)
    middle_im = (cos_part[:, :, length:] - orient * sin_part[:, :, :length]).astype(jnp.bfloat16)
    stacked = jnp.concatenate([middle_re, middle_im], axis=1)
    cos_part = jnp.einsum("mij,jk->mik", stacked, cos_table, preferred_element_type=jnp.float32)
    sin_part = jnp.einsum("mij,jk->mik", stacked, sin_table, preferred_element_type=jnp.float32)
    result_re = cos_part[:, :length] + orient * sin_part[:, length:]
    result_im = cos_part[:, length:] - orient * sin_part[:, :length]
    return (result_re, result_im)


def slot_terms(window, probe_modes, measured, alive_mask, cos_table, sin_table):
    window_re, window_im = (window[0], window[1])
    probe_re, probe_im = (probe_modes[0], probe_modes[1])
    wave_re = (probe_re * window_re - probe_im * window_im).astype(jnp.bfloat16)
    wave_im = (probe_re * window_im + probe_im * window_re).astype(jnp.bfloat16)
    far_re, far_im = transform(wave_re, wave_im, cos_table, sin_table, 1.0)
    intensity = jnp.sum(far_re * far_re + far_im * far_im, axis=0)
    factor = measured * lax.rsqrt(jnp.maximum(intensity, 1.0)) - 1.0
    delta_re = (far_re * factor).astype(jnp.bfloat16)
    delta_im = (far_im * factor).astype(jnp.bfloat16)
    back_re, back_im = transform(delta_re, delta_im, cos_table, sin_table, -1.0)
    back_re = back_re * alive_mask
    back_im = back_im * alive_mask
    grad_re = jnp.sum(probe_re * back_re + probe_im * back_im, axis=0)
    grad_im = jnp.sum(probe_re * back_im - probe_im * back_re, axis=0)
    mode_re = window_re * back_re + window_im * back_im
    mode_im = window_re * back_im - window_im * back_re
    return (jnp.stack([grad_re, grad_im]), jnp.stack([mode_re, mode_im]))


def shifted(value, axis, pairs):
    return lax.ppermute(value, axis, [(a, b) for a, b in pairs if 0 <= b < lax.axis_size(axis)])


def local(specimen, probe_modes, amplitude, offsets, live_slots):
    tile_h = specimen.shape[1]
    width = probe_modes.shape[2]
    slots = live_slots.shape[0]
    devices_all = lax.axis_size(TY) * lax.axis_size(TX)
    count = lax.axis_size(TX)
    evens = range(0, count, 2)
    odds = range(1, count, 2)
    anchor = jnp.zeros((), jnp.int32)
    cos_table, sin_table = tables(width)

    alive_own = live_slots.astype(jnp.float32)
    live_count = jnp.sum(alive_own)
    got_measured, got_count, got_offset = partner((amplitude[1:], live_count, offsets[1]), TX, 0)
    use_own = live_count >= 1.0
    is_odd = lax.axis_index(TX) % 2 == 1
    shift = jnp.where(use_own, 0, jnp.where(is_odd, -1, 1))
    row_at = jnp.where(use_own, offsets[0, 0], got_offset[0])
    col_at = jnp.where(use_own, offsets[0, 1], got_offset[1])
    measured = jnp.where(use_own, amplitude[0], got_measured[0])
    alive = jnp.where(use_own, alive_own[0], (1.0 < got_count).astype(jnp.float32))

    row_left = shifted(row_at, TX, [(s, s + 1) for s in range(count)])
    row_right = shifted(row_at, TX, [(s, s - 1) for s in range(count)])
    row_left2 = shifted(row_at, TX, [(s, s + 2) for s in evens])

    below = passed_along(specimen[:, :width, :], TY, -1)
    column = jnp.concatenate([specimen, below], axis=1)

    def strip(source, at):
        return lax.dynamic_slice(source, (anchor, at, anchor), (2, width, width))

    own_strip = strip(column, row_at)
    from_right = shifted(strip(column, row_left), TX, [(s, s - 1) for s in range(count)])
    from_left = shifted(strip(column, row_right), TX, [(s, s + 1) for s in evens])
    from_right2 = shifted(strip(column, row_left2), TX, [(s, s - 2) for s in evens])
    left_strip = jnp.where(shift == 0, own_strip, jnp.where(shift < 0, from_left, from_right))
    right_strip = jnp.where(shift == 0, from_right, jnp.where(shift < 0, own_strip, from_right2))
    pair_strip = jnp.concatenate([left_strip, right_strip], axis=2)
    window = lax.dynamic_slice(pair_strip, (anchor, anchor, col_at), (2, width, width))

    grad_term, probe_term = slot_terms(window, probe_modes, measured, alive, cos_table, sin_table)

    probe_grad = all_sum(probe_term, ("ty_1", "ty_0", "tx_0", "tx_1"), 1.0 / math.sqrt(slots * devices_all))

    placed = lax.dynamic_slice(
        jnp.pad(grad_term, ((0, 0), (0, 0), (width, width))), (anchor, anchor, width - col_at), (2, width, 2 * width)
    )
    grad_left = placed[:, :, :width]
    grad_right = placed[:, :, width:]
    zeros = jnp.zeros_like(grad_left)
    send_right = jnp.where(shift == 0, grad_right, jnp.where(shift > 0, grad_left, zeros))
    send_right2 = jnp.where(shift > 0, grad_right, zeros)
    send_left = jnp.where(shift < 0, grad_left, zeros)
    keep = jnp.where(shift == 0, grad_left, jnp.where(shift < 0, grad_right, zeros))
    got_left = shifted(send_right, TX, [(s, s + 1) for s in range(count)])
    got_left2 = shifted(send_right2, TX, [(s, s + 2) for s in evens])
    got_right = shifted(send_left, TX, [(s, s - 1) for s in odds])

    rows_all = column.shape[1]

    def spread(piece, at):
        padded = jnp.pad(piece, ((0, 0), (rows_all, rows_all), (0, 0)))
        return lax.dynamic_slice(padded, (anchor, rows_all - at, anchor), (2, rows_all, width))

    grad_column = (
        (spread(keep, row_at) + spread(got_left, row_left)) + spread(got_left2, row_left2)
    ) + spread(got_right, row_right)
    from_above = passed_along(grad_column[:, tile_h:, :], TY, 1)
    core_grad = grad_column[:, :tile_h, :].at[:, :width, :].add(from_above)
    return (core_grad, probe_grad)


def solution(mesh):
    finer = Mesh(mesh.devices.reshape(4, 2, 4, 4), ("ty_0", "ty_1", "tx_0", "tx_1"))
    placed = (P(None, TY, TX), P(), P(TY_TX, None, None), P(TY_TX, None), P(TY_TX))

    return jax.shard_map(
        local, mesh=finer, in_specs=placed, out_specs=(P(None, TY, TX), P()), check_vma=False
    )
```

```python
import math

import jax
import jax.numpy as jnp
from jax import lax
from jax.sharding import Mesh
from jax.sharding import PartitionSpec as P


TY = ("ty_0", "ty_1")
TX = ("tx_0", "tx_1")
TY_TX = ("ty_0", "ty_1", "tx_0", "tx_1")


def passed_along(value, axis, steps):
    count = lax.axis_size(axis)
    initial, last = (max(0, -steps), min(count, count - steps))
    return lax.ppermute(value, axis, [(source, source + steps) for source in range(initial, last)])


def partner(value, axis, apart):
    mask = 2**apart
    pairs = [(source, source ^ mask) for source in range(lax.axis_size(axis))]
    return lax.ppermute(value, axis, pairs)


def scatter_axis(lines, axis):
    count = lax.axis_size(axis)
    me = lax.axis_index(axis)
    chunks = lines.reshape(count, -1, lines.shape[-1])
    total = lax.dynamic_index_in_dim(chunks, me, keepdims=False)
    for step in range(1, count):
        sent = lax.dynamic_index_in_dim(chunks, (me + step) % count, keepdims=False)
        pairs = [(source, (source + step) % count) for source in range(count)]
        total = total + lax.ppermute(sent, axis, pairs)
    return total


def all_sum(value, axes, scale):
    lines = value.reshape(-1, value.shape[-1])
    for axis in axes:
        lines = scatter_axis(lines, axis)
    lines = lines * scale
    lines = lax.all_gather(lines, tuple(axes), tiled=True)
    return lines.reshape(value.shape)


def tables(length):
    index = jnp.arange(length, dtype=jnp.int32)
    phase = index[:, None] * index[None, :] % length
    angle = phase.astype(jnp.float32) * (2.0 * math.pi / length)
    scale = 1.0 / math.sqrt(length)
    return (
        (jnp.cos(angle) * scale).astype(jnp.bfloat16),
        (jnp.sin(angle) * scale).astype(jnp.bfloat16),
    )


def transform(real_part, imag_part, cos_table, sin_table, orient):
    length = real_part.shape[-1]
    stacked = jnp.concatenate([real_part, imag_part], axis=2)
    cos_part = jnp.einsum("ij,mjk->mik", cos_table, stacked, preferred_element_type=jnp.float32)
    sin_part = jnp.einsum("ij,mjk->mik", sin_table, stacked, preferred_element_type=jnp.float32)
    middle_re = (cos_part[:, :, :length] + orient * sin_part[:, :, length:]).astype(jnp.bfloat16)
    middle_im = (cos_part[:, :, length:] - orient * sin_part[:, :, :length]).astype(jnp.bfloat16)
    stacked = jnp.concatenate([middle_re, middle_im], axis=1)
    cos_part = jnp.einsum("mij,jk->mik", stacked, cos_table, preferred_element_type=jnp.float32)
    sin_part = jnp.einsum("mij,jk->mik", stacked, sin_table, preferred_element_type=jnp.float32)
    result_re = cos_part[:, :length] + orient * sin_part[:, length:]
    result_im = cos_part[:, length:] - orient * sin_part[:, :length]
    return (result_re, result_im)


def slot_terms(window, probe_modes, measured, alive_mask, cos_table, sin_table):
    window_re, window_im = (window[0], window[1])
    probe_re, probe_im = (probe_modes[0], probe_modes[1])
    wave_re = (probe_re * window_re - probe_im * window_im).astype(jnp.bfloat16)
    wave_im = (probe_re * window_im + probe_im * window_re).astype(jnp.bfloat16)
    far_re, far_im = transform(wave_re, wave_im, cos_table, sin_table, 1.0)
    intensity = jnp.sum(far_re * far_re + far_im * far_im, axis=0)
    factor = measured * lax.rsqrt(jnp.maximum(intensity, 1.0)) - 1.0
    delta_re = (far_re * factor).astype(jnp.bfloat16)
    delta_im = (far_im * factor).astype(jnp.bfloat16)
    back_re, back_im = transform(delta_re, delta_im, cos_table, sin_table, -1.0)
    back_re = back_re * alive_mask
    back_im = back_im * alive_mask
    grad_re = jnp.sum(probe_re * back_re + probe_im * back_im, axis=0)
    grad_im = jnp.sum(probe_re * back_im - probe_im * back_re, axis=0)
    mode_re = window_re * back_re + window_im * back_im
    mode_im = window_re * back_im - window_im * back_re
    return (jnp.stack([grad_re, grad_im]), jnp.stack([mode_re, mode_im]))


def shifted(value, axis, pairs):
    return lax.ppermute(value, axis, [(a, b) for a, b in pairs if 0 <= b < lax.axis_size(axis)])


def local(specimen, probe_modes, amplitude, offsets, live_slots):
    tile_h = specimen.shape[1]
    width = probe_modes.shape[2]
    slots = live_slots.shape[0]
    devices_all = lax.axis_size(TY) * lax.axis_size(TX)
    count = lax.axis_size(TX)
    evens = range(0, count, 2)
    odds = range(1, count, 2)
    anchor = jnp.zeros((), jnp.int32)
    cos_table, sin_table = tables(width)

    alive_own = live_slots.astype(jnp.float32)
    live_count = jnp.sum(alive_own)
    got_measured = partner(amplitude[1:], TX, 0)
    info = jnp.concatenate([jnp.sum(live_slots)[None], offsets[0], offsets[1]])
    info_l1 = shifted(info, TX, [(s, s + 1) for s in range(count)])
    info_r1 = shifted(info, TX, [(s, s - 1) for s in range(count)])
    info_l2 = shifted(info, TX, [(s, s + 2) for s in range(count)])
    info_r2 = shifted(info, TX, [(s, s - 2) for s in range(count)])
    is_odd = lax.axis_index(TX) % 2 == 1

    def processed_row(own, other):
        return jnp.where(own[0] >= 1, own[1], other[3])

    got_info = jnp.where(is_odd, info_l1, info_r1)
    use_own = live_count >= 1.0
    shift = jnp.where(use_own, 0, jnp.where(is_odd, -1, 1))
    row_at = jnp.where(use_own, offsets[0, 0], got_info[3])
    col_at = jnp.where(use_own, offsets[0, 1], got_info[4])
    measured = jnp.where(use_own, amplitude[0], got_measured[0])
    alive = jnp.where(use_own, alive_own[0], (1 < got_info[0]).astype(jnp.float32))

    row_left = processed_row(info_l1, jnp.where(is_odd, info, info_l2))
    row_right = processed_row(info_r1, jnp.where(is_odd, info_r2, info))
    row_left2 = processed_row(info_l2, info_l1)

    below = passed_along(specimen[:, :width, :], TY, -1)
    column = jnp.concatenate([specimen, below], axis=1)

    def strip(source, at):
        return lax.dynamic_slice(source, (anchor, at, anchor), (2, width, width))

    own_strip = strip(column, row_at)
    from_right = shifted(strip(column, row_left), TX, [(s, s - 1) for s in range(count)])
    from_left = shifted(strip(column, row_right), TX, [(s, s + 1) for s in evens])
    from_right2 = shifted(strip(column, row_left2), TX, [(s, s - 2) for s in evens])
    left_strip = jnp.where(shift == 0, own_strip, jnp.where(shift < 0, from_left, from_right))
    right_strip = jnp.where(shift == 0, from_right, jnp.where(shift < 0, own_strip, from_right2))
    pair_strip = jnp.concatenate([left_strip, right_strip], axis=2)
    window = lax.dynamic_slice(pair_strip, (anchor, anchor, col_at), (2, width, width))

    grad_term, probe_term = slot_terms(window, probe_modes, measured, alive, cos_table, sin_table)

    probe_grad = all_sum(probe_term, ("ty_1", "ty_0", "tx_0", "tx_1"), 1.0 / math.sqrt(slots * devices_all))

    placed = lax.dynamic_slice(
        jnp.pad(grad_term, ((0, 0), (0, 0), (width, width))), (anchor, anchor, width - col_at), (2, width, 2 * width)
    )
    grad_left = placed[:, :, :width]
    grad_right = placed[:, :, width:]
    zeros = jnp.zeros_like(grad_left)
    send_right = jnp.where(shift == 0, grad_right, jnp.where(shift > 0, grad_left, zeros))
    send_right2 = jnp.where(shift > 0, grad_right, zeros)
    send_left = jnp.where(shift < 0, grad_left, zeros)
    keep = jnp.where(shift == 0, grad_left, jnp.where(shift < 0, grad_right, zeros))
    got_left = shifted(send_right, TX, [(s, s + 1) for s in range(count)])
    got_left2 = shifted(send_right2, TX, [(s, s + 2) for s in evens])
    got_right = shifted(send_left, TX, [(s, s - 1) for s in odds])

    rows_all = column.shape[1]

    def spread(piece, at):
        padded = jnp.pad(piece, ((0, 0), (rows_all, rows_all), (0, 0)))
        return lax.dynamic_slice(padded, (anchor, rows_all - at, anchor), (2, rows_all, width))

    grad_column = (
        (spread(keep, row_at) + spread(got_left, row_left)) + spread(got_left2, row_left2)
    ) + spread(got_right, row_right)
    from_above = passed_along(grad_column[:, tile_h:, :], TY, 1)
    core_grad = grad_column[:, :tile_h, :].at[:, :width, :].add(from_above)
    return (core_grad, probe_grad)


def solution(mesh):
    finer = Mesh(mesh.devices.reshape(4, 2, 4, 4), ("ty_0", "ty_1", "tx_0", "tx_1"))
    placed = (P(None, TY, TX), P(), P(TY_TX, None, None), P(TY_TX, None), P(TY_TX))

    return jax.shard_map(
        local, mesh=finer, in_specs=placed, out_specs=(P(None, TY, TX), P()), check_vma=False
    )
```

```python
import math

import jax
import jax.numpy as jnp
from jax import lax
from jax.sharding import Mesh
from jax.sharding import PartitionSpec as P


TY = ("ty_0", "ty_1")
TX = ("tx_0", "tx_1")
TY_TX = ("ty_0", "ty_1", "tx_0", "tx_1")


def passed_along(value, axis, steps):
    count = lax.axis_size(axis)
    initial, last = (max(0, -steps), min(count, count - steps))
    return lax.ppermute(value, axis, [(source, source + steps) for source in range(initial, last)])


def partner(value, axis, apart):
    mask = 2**apart
    pairs = [(source, source ^ mask) for source in range(lax.axis_size(axis))]
    return lax.ppermute(value, axis, pairs)


def scatter_axis(lines, axis):
    count = lax.axis_size(axis)
    me = lax.axis_index(axis)
    chunks = lines.reshape(count, -1, lines.shape[-1])
    total = lax.dynamic_index_in_dim(chunks, me, keepdims=False)
    for step in range(1, count):
        sent = lax.dynamic_index_in_dim(chunks, (me + step) % count, keepdims=False)
        pairs = [(source, (source + step) % count) for source in range(count)]
        total = total + lax.ppermute(sent, axis, pairs)
    return total


def all_sum(value, axes, scale):
    lines = value.reshape(-1, value.shape[-1])
    for axis in axes:
        lines = scatter_axis(lines, axis)
    lines = lines * scale
    lines = lax.all_gather(lines, tuple(axes), tiled=True)
    return lines.reshape(value.shape)


def tables(length):
    index = jnp.arange(length, dtype=jnp.int32)
    phase = index[:, None] * index[None, :] % length
    angle = phase.astype(jnp.float32) * (2.0 * math.pi / length)
    scale = 1.0 / math.sqrt(length)
    return (
        (jnp.cos(angle) * scale).astype(jnp.bfloat16),
        (jnp.sin(angle) * scale).astype(jnp.bfloat16),
    )


def transform(real_part, imag_part, cos_table, sin_table, orient):
    length = real_part.shape[-1]
    stacked = jnp.concatenate([real_part, imag_part], axis=2)
    cos_part = jnp.einsum("ij,mjk->mik", cos_table, stacked, preferred_element_type=jnp.float32)
    sin_part = jnp.einsum("ij,mjk->mik", sin_table, stacked, preferred_element_type=jnp.float32)
    middle_re = (cos_part[:, :, :length] + orient * sin_part[:, :, length:]).astype(jnp.bfloat16)
    middle_im = (cos_part[:, :, length:] - orient * sin_part[:, :, :length]).astype(jnp.bfloat16)
    stacked = jnp.concatenate([middle_re, middle_im], axis=1)
    cos_part = jnp.einsum("mij,jk->mik", stacked, cos_table, preferred_element_type=jnp.float32)
    sin_part = jnp.einsum("mij,jk->mik", stacked, sin_table, preferred_element_type=jnp.float32)
    result_re = cos_part[:, :length] + orient * sin_part[:, length:]
    result_im = cos_part[:, length:] - orient * sin_part[:, :length]
    return (result_re, result_im)


def slot_terms(window, probe_modes, measured, alive_mask, cos_table, sin_table):
    window_re, window_im = (window[0], window[1])
    probe_re, probe_im = (probe_modes[0], probe_modes[1])
    wave_re = (probe_re * window_re - probe_im * window_im).astype(jnp.bfloat16)
    wave_im = (probe_re * window_im + probe_im * window_re).astype(jnp.bfloat16)
    far_re, far_im = transform(wave_re, wave_im, cos_table, sin_table, 1.0)
    intensity = jnp.sum(far_re * far_re + far_im * far_im, axis=0)
    factor = measured * lax.rsqrt(jnp.maximum(intensity, 1.0)) - 1.0
    delta_re = (far_re * factor).astype(jnp.bfloat16)
    delta_im = (far_im * factor).astype(jnp.bfloat16)
    back_re, back_im = transform(delta_re, delta_im, cos_table, sin_table, -1.0)
    back_re = back_re * alive_mask
    back_im = back_im * alive_mask
    grad_re = jnp.sum(probe_re * back_re + probe_im * back_im, axis=0)
    grad_im = jnp.sum(probe_re * back_im - probe_im * back_re, axis=0)
    mode_re = window_re * back_re + window_im * back_im
    mode_im = window_re * back_im - window_im * back_re
    return (jnp.stack([grad_re, grad_im]), jnp.stack([mode_re, mode_im]))


def shifted(value, axis, pairs):
    return lax.ppermute(value, axis, [(a, b) for a, b in pairs if 0 <= b < lax.axis_size(axis)])


def local(specimen, probe_modes, amplitude, offsets, live_slots):
    tile_h = specimen.shape[1]
    width = probe_modes.shape[2]
    slots = live_slots.shape[0]
    devices_all = lax.axis_size(TY) * lax.axis_size(TX)
    count = lax.axis_size(TX)
    evens = range(0, count, 2)
    odds = range(1, count, 2)
    anchor = jnp.zeros((), jnp.int32)
    cos_table, sin_table = tables(width)

    alive_own = live_slots.astype(jnp.float32)
    live_count = jnp.sum(alive_own)
    got_measured = partner(amplitude[1:], TX, 0)
    info = jnp.concatenate([jnp.sum(live_slots)[None], offsets[0], offsets[1]])
    info_l1 = shifted(info, TX, [(s, s + 1) for s in range(count)])
    info_r1 = shifted(info, TX, [(s, s - 1) for s in range(count)])
    info_l2 = shifted(info, TX, [(s, s + 2) for s in range(count)])
    info_r2 = shifted(info, TX, [(s, s - 2) for s in range(count)])
    is_odd = lax.axis_index(TX) % 2 == 1

    def processed_row(own, other):
        return jnp.where(own[0] >= 1, own[1], other[3])

    got_info = jnp.where(is_odd, info_l1, info_r1)
    use_own = live_count >= 1.0
    shift = jnp.where(use_own, 0, jnp.where(is_odd, -1, 1))
    row_at = jnp.where(use_own, offsets[0, 0], got_info[3])
    col_at = jnp.where(use_own, offsets[0, 1], got_info[4])
    measured = jnp.where(use_own, amplitude[0], got_measured[0])
    alive = jnp.where(use_own, alive_own[0], (1 < got_info[0]).astype(jnp.float32))

    row_left = processed_row(info_l1, jnp.where(is_odd, info, info_l2))
    row_right = processed_row(info_r1, jnp.where(is_odd, info_r2, info))
    row_left2 = processed_row(info_l2, info_l1)

    half = width // 2
    below_first = passed_along(specimen[:, :width, :half], TY, -1)
    second_cols, below_first = lax.optimization_barrier((specimen[:, :width, half:], below_first))
    below_second = passed_along(second_cols, TY, -1)

    def strips(column):
        def strip(at):
            return lax.dynamic_slice(column, (anchor, at, anchor), (2, width, column.shape[2]))

        own_strip = strip(row_at)
        from_right = shifted(strip(row_left), TX, [(s, s - 1) for s in range(count)])
        from_left = shifted(strip(row_right), TX, [(s, s + 1) for s in evens])
        from_right2 = shifted(strip(row_left2), TX, [(s, s - 2) for s in evens])
        left_strip = jnp.where(shift == 0, own_strip, jnp.where(shift < 0, from_left, from_right))
        right_strip = jnp.where(shift == 0, from_right, jnp.where(shift < 0, own_strip, from_right2))
        return left_strip, right_strip

    left_first, right_first = strips(jnp.concatenate([specimen[:, :, :half], below_first], axis=1))
    left_second, right_second = strips(jnp.concatenate([specimen[:, :, half:], below_second], axis=1))
    left_strip = jnp.concatenate([left_first, left_second], axis=2)
    right_strip = jnp.concatenate([right_first, right_second], axis=2)
    pair_strip = jnp.concatenate([left_strip, right_strip], axis=2)
    window = lax.dynamic_slice(pair_strip, (anchor, anchor, col_at), (2, width, width))

    grad_term, probe_term = slot_terms(window, probe_modes, measured, alive, cos_table, sin_table)

    probe_grad = all_sum(probe_term, ("ty_1", "ty_0", "tx_0", "tx_1"), 1.0 / math.sqrt(slots * devices_all))

    placed = lax.dynamic_slice(
        jnp.pad(grad_term, ((0, 0), (0, 0), (width, width))), (anchor, anchor, width - col_at), (2, width, 2 * width)
    )
    grad_left = placed[:, :, :width]
    grad_right = placed[:, :, width:]
    zeros = jnp.zeros_like(grad_left)
    send_right = jnp.where(shift == 0, grad_right, jnp.where(shift > 0, grad_left, zeros))
    send_right2 = jnp.where(shift > 0, grad_right, zeros)
    send_left = jnp.where(shift < 0, grad_left, zeros)
    keep = jnp.where(shift == 0, grad_left, jnp.where(shift < 0, grad_right, zeros))
    got_left = shifted(send_right, TX, [(s, s + 1) for s in range(count)])
    got_left2 = shifted(send_right2, TX, [(s, s + 2) for s in evens])
    got_right = shifted(send_left, TX, [(s, s - 1) for s in odds])

    def spread(piece, at):
        padded = jnp.pad(piece, ((0, 0), (rows_all, rows_all), (0, 0)))
        return lax.dynamic_slice(padded, (anchor, rows_all - at, anchor), (2, rows_all, width))

    rows_all = tile_h + width
    grad_column = (
        (spread(keep, row_at) + spread(got_left, row_left)) + spread(got_left2, row_left2)
    ) + spread(got_right, row_right)
    from_above = passed_along(grad_column[:, tile_h:, :], TY, 1)
    core_grad = grad_column[:, :tile_h, :].at[:, :width, :].add(from_above)
    return (core_grad, probe_grad)


def solution(mesh):
    finer = Mesh(mesh.devices.reshape(4, 2, 4, 4), ("ty_0", "ty_1", "tx_0", "tx_1"))
    placed = (P(None, TY, TX), P(), P(TY_TX, None, None), P(TY_TX, None), P(TY_TX))

    return jax.shard_map(
        local, mesh=finer, in_specs=placed, out_specs=(P(None, TY, TX), P()), check_vma=False
    )
```

```python
import math

import jax
import jax.numpy as jnp
from jax import lax
from jax.sharding import Mesh
from jax.sharding import PartitionSpec as P


TY = ("ty_0", "ty_1")
TX = ("tx_0", "tx_1")
TY_TX = ("ty_0", "ty_1", "tx_0", "tx_1")


def passed_along(value, axis, steps):
    count = lax.axis_size(axis)
    initial, last = (max(0, -steps), min(count, count - steps))
    return lax.ppermute(value, axis, [(source, source + steps) for source in range(initial, last)])


def partner(value, axis, apart):
    mask = 2**apart
    pairs = [(source, source ^ mask) for source in range(lax.axis_size(axis))]
    return lax.ppermute(value, axis, pairs)


def scatter_axis(lines, axis):
    count = lax.axis_size(axis)
    me = lax.axis_index(axis)
    chunks = lines.reshape(count, -1, lines.shape[-1])
    total = lax.dynamic_index_in_dim(chunks, me, keepdims=False)
    for step in range(1, count):
        sent = lax.dynamic_index_in_dim(chunks, (me + step) % count, keepdims=False)
        pairs = [(source, (source + step) % count) for source in range(count)]
        total = total + lax.ppermute(sent, axis, pairs)
    return total


def all_sum(value, axes, scale):
    lines = value.reshape(-1, value.shape[-1])
    for axis in axes:
        lines = scatter_axis(lines, axis)
    lines = lines * scale
    lines = lax.all_gather(lines, tuple(axes), tiled=True)
    return lines.reshape(value.shape)


def tables(length):
    index = jnp.arange(length, dtype=jnp.int32)
    phase = index[:, None] * index[None, :] % length
    angle = phase.astype(jnp.float32) * (2.0 * math.pi / length)
    scale = 1.0 / math.sqrt(length)
    return (
        (jnp.cos(angle) * scale).astype(jnp.bfloat16),
        (jnp.sin(angle) * scale).astype(jnp.bfloat16),
    )


def transform(real_part, imag_part, cos_table, sin_table, orient):
    length = real_part.shape[-1]
    stacked = jnp.concatenate([real_part, imag_part], axis=2)
    both = jnp.einsum(
        "ij,mjk->mik", jnp.concatenate([cos_table, sin_table], axis=0), stacked, preferred_element_type=jnp.float32
    )
    cos_part = both[:, :length, :]
    sin_part = both[:, length:, :]
    middle_re = (cos_part[:, :, :length] + orient * sin_part[:, :, length:]).astype(jnp.bfloat16)
    middle_im = (cos_part[:, :, length:] - orient * sin_part[:, :, :length]).astype(jnp.bfloat16)
    stacked = jnp.concatenate([middle_re, middle_im], axis=1)
    both = jnp.einsum(
        "mij,jk->mik", stacked, jnp.concatenate([cos_table, sin_table], axis=1), preferred_element_type=jnp.float32
    )
    cos_part = both[:, :, :length]
    sin_part = both[:, :, length:]
    result_re = cos_part[:, :length] + orient * sin_part[:, length:]
    result_im = cos_part[:, length:] - orient * sin_part[:, :length]
    return (result_re, result_im)


def slot_terms(window, probe_modes, measured, alive_mask, cos_table, sin_table):
    window_re, window_im = (window[0], window[1])
    probe_re, probe_im = (probe_modes[0], probe_modes[1])
    wave_re = (probe_re * window_re - probe_im * window_im).astype(jnp.bfloat16)
    wave_im = (probe_re * window_im + probe_im * window_re).astype(jnp.bfloat16)
    far_re, far_im = transform(wave_re, wave_im, cos_table, sin_table, 1.0)
    intensity = jnp.sum(far_re * far_re + far_im * far_im, axis=0)
    factor = measured * lax.rsqrt(jnp.maximum(intensity, 1.0)) - 1.0
    delta_re = (far_re * factor).astype(jnp.bfloat16)
    delta_im = (far_im * factor).astype(jnp.bfloat16)
    back_re, back_im = transform(delta_re, delta_im, cos_table, sin_table, -1.0)
    back_re = back_re * alive_mask
    back_im = back_im * alive_mask
    grad_re = jnp.sum(probe_re * back_re + probe_im * back_im, axis=0)
    grad_im = jnp.sum(probe_re * back_im - probe_im * back_re, axis=0)
    mode_re = window_re * back_re + window_im * back_im
    mode_im = window_re * back_im - window_im * back_re
    return (jnp.stack([grad_re, grad_im]), jnp.stack([mode_re, mode_im]))


def shifted(value, axis, pairs):
    return lax.ppermute(value, axis, [(a, b) for a, b in pairs if 0 <= b < lax.axis_size(axis)])


def local(specimen, probe_modes, amplitude, offsets, live_slots):
    tile_h = specimen.shape[1]
    width = probe_modes.shape[2]
    slots = live_slots.shape[0]
    devices_all = lax.axis_size(TY) * lax.axis_size(TX)
    count = lax.axis_size(TX)
    evens = range(0, count, 2)
    odds = range(1, count, 2)
    anchor = jnp.zeros((), jnp.int32)
    cos_table, sin_table = tables(width)

    alive_own = live_slots.astype(jnp.float32)
    live_count = jnp.sum(alive_own)
    got_measured = partner(amplitude[1:], TX, 0)
    info = jnp.concatenate([jnp.sum(live_slots)[None], offsets[0], offsets[1]])
    info_l1 = shifted(info, TX, [(s, s + 1) for s in range(count)])
    info_r1 = shifted(info, TX, [(s, s - 1) for s in range(count)])
    info_l2 = shifted(info, TX, [(s, s + 2) for s in range(count)])
    info_r2 = shifted(info, TX, [(s, s - 2) for s in range(count)])
    is_odd = lax.axis_index(TX) % 2 == 1

    def processed_row(own, other):
        return jnp.where(own[0] >= 1, own[1], other[3])

    got_info = jnp.where(is_odd, info_l1, info_r1)
    use_own = live_count >= 1.0
    shift = jnp.where(use_own, 0, jnp.where(is_odd, -1, 1))
    row_at = jnp.where(use_own, offsets[0, 0], got_info[3])
    col_at = jnp.where(use_own, offsets[0, 1], got_info[4])
    measured = jnp.where(use_own, amplitude[0], got_measured[0])
    alive = jnp.where(use_own, alive_own[0], (1 < got_info[0]).astype(jnp.float32))

    row_left = processed_row(info_l1, jnp.where(is_odd, info, info_l2))
    row_right = processed_row(info_r1, jnp.where(is_odd, info_r2, info))
    row_left2 = processed_row(info_l2, info_l1)

    below = passed_along(specimen[:, :width, :], TY, -1)
    column = jnp.concatenate([specimen, below], axis=1)
    column, got_measured = lax.optimization_barrier((column, got_measured))

    def strip(source, at):
        return lax.dynamic_slice(source, (anchor, at, anchor), (2, width, width))

    own_strip = strip(column, row_at)
    from_right = shifted(strip(column, row_left), TX, [(s, s - 1) for s in range(count)])
    from_left = shifted(strip(column, row_right), TX, [(s, s + 1) for s in evens])
    from_right2 = shifted(strip(column, row_left2), TX, [(s, s - 2) for s in evens])
    left_strip = jnp.where(shift == 0, own_strip, jnp.where(shift < 0, from_left, from_right))
    right_strip = jnp.where(shift == 0, from_right, jnp.where(shift < 0, own_strip, from_right2))
    pair_strip = jnp.concatenate([left_strip, right_strip], axis=2)
    window = lax.dynamic_slice(pair_strip, (anchor, anchor, col_at), (2, width, width))

    grad_term, probe_term = slot_terms(window, probe_modes, measured, alive, cos_table, sin_table)

    probe_grad = all_sum(probe_term, ("ty_1", "ty_0", "tx_0", "tx_1"), 1.0 / math.sqrt(slots * devices_all))

    placed = lax.dynamic_slice(
        jnp.pad(grad_term, ((0, 0), (0, 0), (width, width))), (anchor, anchor, width - col_at), (2, width, 2 * width)
    )
    grad_left = placed[:, :, :width]
    grad_right = placed[:, :, width:]
    zeros = jnp.zeros_like(grad_left)
    send_right = jnp.where(shift == 0, grad_right, jnp.where(shift > 0, grad_left, zeros))
    send_right2 = jnp.where(shift > 0, grad_right, zeros)
    send_left = jnp.where(shift < 0, grad_left, zeros)
    keep = jnp.where(shift == 0, grad_left, jnp.where(shift < 0, grad_right, zeros))
    got_left = shifted(send_right, TX, [(s, s + 1) for s in range(count)])
    got_left2 = shifted(send_right2, TX, [(s, s + 2) for s in evens])
    got_right = shifted(send_left, TX, [(s, s - 1) for s in odds])

    rows_all = column.shape[1]

    def spread(piece, at):
        padded = jnp.pad(piece, ((0, 0), (rows_all, rows_all), (0, 0)))
        return lax.dynamic_slice(padded, (anchor, rows_all - at, anchor), (2, rows_all, width))

    grad_column = (
        (spread(keep, row_at) + spread(got_left, row_left)) + spread(got_left2, row_left2)
    ) + spread(got_right, row_right)
    from_above = passed_along(grad_column[:, tile_h:, :], TY, 1)
    core_grad = grad_column[:, :tile_h, :].at[:, :width, :].add(from_above)
    return (core_grad, probe_grad)


def solution(mesh):
    finer = Mesh(mesh.devices.reshape(4, 2, 4, 4), ("ty_0", "ty_1", "tx_0", "tx_1"))
    placed = (P(None, TY, TX), P(), P(TY_TX, None, None), P(TY_TX, None), P(TY_TX))

    return jax.shard_map(
        local, mesh=finer, in_specs=placed, out_specs=(P(None, TY, TX), P()), check_vma=False
    )
```
